256 devices in a mesh: blk: 32 (over y_hi, z, core), pair: 8 (over y_lo, x).
Axes of the slice: x: 4, y: 4 (y_hi: 2, y_lo: 2; y = y_hi * 2 + y_lo), z: 8, core: 2. Of those that a mesh axis runs over, the one named last changes fastest.
Arguments:
- particles: float32 [262144, 512], P(('blk', 'pair'))
- log_prior: float32 [262144], P(('blk', 'pair'))
- transition: bfloat16 [512, 512], replicated, may hold values from -0.25 to 0.25
- drive_vector: float32 [512], replicated, may hold values from -3 to 3
- current: float32 [4], replicated, may hold values from -4 to 4
- decay_rate: float32 [512], replicated, may hold values from 0.3 to 0.98
- obs_matrix: bfloat16 [512, 128], replicated, may hold values from -0.25 to 0.25
- obs_weight: float32 [128], replicated, may hold values from 0.05 to 0.5
- observed: float32 [4, 128], replicated
- ancestors: int32 [262144], P(('blk', 'pair')), may hold values from 0 to 1023
- cycle_pick: int32 [65536], P(('blk', 'pair')), may hold values from 0 to 1023, as said below
- pair_pick: int32 [8192], P(('blk', 'pair')), may hold values from 0 to 1023, as said below
Outputs:
- migrated: float32 [262144, 512], P(('blk', 'pair'))
- group_logw: float32 [262144], P(('blk', 'pair'))
- mean_state: float32 [512], replicated
The draws below stay inside these ranges and needn't reach their ends.
Inputs may be any that keep to these rules, and one draw needn't show every extreme that they name: On each device, cycle_pick's 256 entries and pair_pick's 32 entries are distinct local positions, none shared between the two. `pair_pick`: distinct local positions, none in the same device's cycle_pick.
All inputs are finite; a program needn't handle non-finite values.
Results may differ from the reference program's by a relative error of at most 0.013.
Values sent between devices are 32-bit elements; how exact they have to be, the bound alone decides.
No kernel may reach another device: no remote copies, remote signals or barrier semaphores. Data moves between devices by JAX's collectives and lax.ppermute only.
A program may use at most 64 MiB of HBM per device.

```python
import math
import jax
import jax.numpy as jnp
from jax import lax

S = 512
OBS = 128
PART_DEV = 1024
STEPS = 4
CYCLE_ROWS = 256
PAIR_ROWS = 32
PARTICLES = 262144
N_BLK = 32
N_PAIR = 8
DEVICES = 256


def draw_particles(key, part):
    common = jax.random.normal(jax.random.fold_in(key, 1), (S,), jnp.float32)
    spread = jax.random.normal(jax.random.fold_in(key, 2), (PARTICLES, S), jnp.float32)
    return common + 0.5 * spread


def draw_log_prior(key, part):
    ramp = 5.0 * jnp.arange(PARTICLES, dtype=jnp.float32) / PARTICLES
    return ramp + 0.5 * jax.random.normal(key, (PARTICLES,), jnp.float32)


def draw_observed(key, part):
    values = jax.random.normal(key, (STEPS, OBS), jnp.float32)
    return values


def pick_tables(key):
    base = jax.random.fold_in(key, 77)
    keys = jax.random.split(base, DEVICES)
    orders = jax.vmap(lambda one_key: jax.random.permutation(one_key, PART_DEV))(keys)
    return orders.astype(jnp.int32)


def draw_cycle_pick(key, part):
    orders = pick_tables(key)
    return orders[:, :CYCLE_ROWS].reshape(-1)


def draw_pair_pick(key, part):
    orders = pick_tables(key)
    return orders[:, CYCLE_ROWS:CYCLE_ROWS + PAIR_ROWS].reshape(-1)


def with_ends(result, stream_key, low, high):
    shape = result.shape
    place = [jax.random.randint(jax.random.fold_in(stream_key, axis), (), 0, shape[axis]) for axis in range(len(shape))]
    result = result.at[tuple(place)].set(low)
    longest = shape.index(max(shape))
    place[longest] = (place[longest] + 1) % shape[longest]
    return result.at[tuple(place)].set(high)


def centred(stream_key, extent, scale, limit, kind=jnp.bfloat16):
    result = jax.random.normal(stream_key, extent, jnp.float32) * scale
    return jnp.minimum(jnp.maximum(result, -limit), limit).astype(kind)


def setup_inputs(seed: int = 0) -> dict:
    splits = jax.random.split(jax.random.key(seed), 13)
    particles = draw_particles(jax.random.fold_in(splits[12], 71), 0)
    log_prior = draw_log_prior(jax.random.fold_in(splits[12], 71), 0)
    transition = centred(splits[2], (S, S), S ** -0.5, 0.25)
    drive_vector = centred(splits[3], (S,), 0.5, 3.0, jnp.float32)
    current = centred(splits[4], (STEPS,), 1.0, 4.0, jnp.float32)
    decay_rate = jnp.clip(jnp.exp(jax.random.uniform(splits[5], (S,), jnp.float32, math.log(0.3), math.log(0.98))), 0.3, 0.98)
    obs_matrix = centred(splits[6], (S, OBS), S ** -0.5, 0.25)
    obs_weight = jnp.clip(jnp.exp(jax.random.uniform(splits[7], (OBS,), jnp.float32, math.log(0.05), math.log(0.5))), 0.05, 0.5)
    observed = draw_observed(jax.random.fold_in(splits[12], 71), 0)
    ancestors = with_ends(jax.random.randint(splits[9], (PARTICLES,), 0, PART_DEV), jax.random.fold_in(splits[9], 1), 0, PART_DEV - 1).astype(jnp.int32)
    cycle_pick = draw_cycle_pick(jax.random.fold_in(splits[12], 71), 0)
    pair_pick = draw_pair_pick(jax.random.fold_in(splits[12], 71), 0)
    return {"particles": particles, "log_prior": log_prior, "transition": transition, "drive_vector": drive_vector, "current": current, "decay_rate": decay_rate, "obs_matrix": obs_matrix, "obs_weight": obs_weight, "observed": observed, "ancestors": ancestors, "cycle_pick": cycle_pick, "pair_pick": pair_pick}


def place_rows(base_rows, cycle_pos, cycle_in, pair_pos, pair_in):
    return base_rows.at[cycle_pos].set(cycle_in).at[pair_pos].set(pair_in)


def reference(particles, log_prior, transition, drive_vector, current, decay_rate, obs_matrix, obs_weight, observed, ancestors, cycle_pick, pair_pick):
    state = particles
    logw = log_prior
    rounded = state.astype(jnp.bfloat16)
    for step_index in range(STEPS):
        drift = jnp.dot(rounded, transition, preferred_element_type=jnp.float32) + current[step_index] * drive_vector
        state = decay_rate * state + jnp.tanh(drift)
        rounded = state.astype(jnp.bfloat16)
        predicted = jnp.dot(rounded, obs_matrix, preferred_element_type=jnp.float32)
        misfit = predicted - observed[step_index]
        logw = logw - 0.5 * jnp.sum(obs_weight * misfit * misfit, axis=1)
    peak = jnp.max(logw)
    expw = jnp.exp(logw - peak)
    total = jnp.sum(expw)
    mean_state = jnp.dot(expw, state, precision=lax.Precision.HIGHEST) / total
    groups = N_BLK * N_PAIR
    dev_sum = jnp.sum(expw.reshape(groups, PART_DEV), axis=1)
    dev_logw = jnp.log(jnp.maximum(groups * dev_sum / total, 0.1))
    states = state.reshape(groups, PART_DEV, S)
    parents = ancestors.reshape(groups, PART_DEV).astype(jnp.int32)
    resampled = jnp.take_along_axis(states, parents[:, :, None], axis=1)
    cycle_pos = cycle_pick.reshape(groups, CYCLE_ROWS)
    pair_pos = pair_pick.reshape(groups, PAIR_ROWS)
    cycle_sent = jnp.take_along_axis(resampled, cycle_pos[:, :, None], axis=1)
    pair_sent = jnp.take_along_axis(resampled, pair_pos[:, :, None], axis=1)
    cycle_in = jnp.roll(cycle_sent.reshape(N_BLK, N_PAIR, CYCLE_ROWS, S), 1, axis=0).reshape(groups, CYCLE_ROWS, S)
    grid_logw = dev_logw.reshape(N_BLK, N_PAIR)
    cycle_w = jnp.roll(grid_logw, 1, axis=0).reshape(groups)
    half_pair = N_PAIR // 2
    pair_in = jnp.roll(pair_sent.reshape(N_BLK, N_PAIR, PAIR_ROWS, S), half_pair, axis=1).reshape(groups, PAIR_ROWS, S)
    pair_w = jnp.roll(grid_logw, half_pair, axis=1).reshape(groups)
    migrated = jax.vmap(place_rows)(resampled, cycle_pos, cycle_in, pair_pos, pair_in)
    base_w = jnp.broadcast_to(dev_logw[:, None], (groups, PART_DEV))
    cycle_wrows = jnp.broadcast_to(cycle_w[:, None], (groups, CYCLE_ROWS))
    pair_wrows = jnp.broadcast_to(pair_w[:, None], (groups, PAIR_ROWS))
    group_logw = jax.vmap(place_rows)(base_w, cycle_pos, cycle_wrows, pair_pos, pair_wrows)
    return migrated.reshape(PARTICLES, S), group_logw.reshape(PARTICLES), mean_state
```

```python
import functools

import jax
import jax.numpy as jnp
from jax import lax
from jax.sharding import Mesh
from jax.sharding import PartitionSpec as P

STEPS = 4
BLK = ("blk_0", "blk_1", "blk_2")
PAIR = ("pair_0", "pair_1")
BLK_PAIR = ("blk_0", "blk_1", "blk_2", "pair_0", "pair_1")


def shifted(block, axis, distance):
    devices = range(lax.axis_size(axis))
    route = [((i - distance) % len(devices), i) for i in devices]
    return lax.ppermute(block, axis, route)


def per_device(
    particles,
    log_prior,
    transition,
    drive_vector,
    current,
    decay_rate,
    obs_matrix,
    obs_weight,
    observed,
    ancestors,
    cycle_pick,
    pair_pick,
):
    state = particles
    logw = log_prior
    rounded = state.astype(jnp.bfloat16)
    for step_index in range(STEPS):
        drift = (
            jnp.dot(rounded, transition, preferred_element_type=jnp.float32)
            + current[step_index] * drive_vector
        )
        state = decay_rate * state + jnp.tanh(drift)
        rounded = state.astype(jnp.bfloat16)
        predicted = jnp.dot(rounded, obs_matrix, preferred_element_type=jnp.float32)
        misfit = predicted - observed[step_index]
        logw = logw - 0.5 * jnp.sum(obs_weight * misfit * misfit, axis=1)
    n_blk = lax.axis_size(BLK)
    n_pair = lax.axis_size(PAIR)
    groups = n_blk * n_pair
    rows_here = state.shape[0]
    n_cycle = cycle_pick.shape[0]
    n_pairs = pair_pick.shape[0]

    cycle_in = shifted(state[ancestors[cycle_pick]], BLK, 1)
    pair_in = shifted(state[ancestors[pair_pick]], PAIR, n_pair // 2)

    peak = lax.pmax(jnp.max(logw), BLK_PAIR)
    expw = jnp.exp(logw - peak)
    local_sum = jnp.sum(expw)
    weighted = jnp.dot(expw, state, precision=lax.Precision.HIGHEST)
    me = lax.axis_index(BLK_PAIR)
    slots = jnp.zeros((groups,), jnp.float32).at[me].set(local_sum)
    summed = lax.psum(jnp.concatenate([slots, weighted]), BLK_PAIR)
    sums = summed[:groups]
    total = jnp.sum(sums)
    mean_state = summed[groups:] / total
    all_logw = jnp.log(jnp.maximum(groups * sums / total, 0.1))

    b = lax.axis_index(BLK)
    p = lax.axis_index(PAIR)
    own_w = all_logw[me]
    cycle_w = all_logw[((b - 1) % n_blk) * n_pair + p]
    pair_w = all_logw[b * n_pair + (p + n_pair // 2) % n_pair]

    source = (
        ancestors.at[cycle_pick]
        .set(rows_here + jnp.arange(n_cycle, dtype=jnp.int32))
        .at[pair_pick]
        .set(rows_here + n_cycle + jnp.arange(n_pairs, dtype=jnp.int32))
    )
    table = jnp.concatenate([state, cycle_in, pair_in], axis=0)
    migrated = table[source]
    group_logw = jnp.where(
        source >= rows_here + n_cycle,
        pair_w,
        jnp.where(source >= rows_here, cycle_w, own_w),
    )
    return (migrated, group_logw, mean_state)


def solution(mesh):
    torus = Mesh(
        mesh.devices.reshape(2, 8, 2, 2, 4), ("blk_0", "blk_1", "blk_2", "pair_0", "pair_1")
    )
    in_specs = (
        P(BLK_PAIR, None),
        P(BLK_PAIR),
        P(),
        P(),
        P(),
        P(),
        P(),
        P(),
        P(),
        P(BLK_PAIR),
        P(BLK_PAIR),
        P(BLK_PAIR),
    )
    out_specs = (P(BLK_PAIR, None), P(BLK_PAIR), P())
    return jax.shard_map(
        per_device, mesh=torus, in_specs=in_specs, out_specs=out_specs, check_vma=False
    )
```

```python
import functools

import jax
import jax.numpy as jnp
from jax import lax
from jax.sharding import Mesh
from jax.sharding import PartitionSpec as P

STEPS = 4
BLK = ("blk_0", "blk_1", "blk_2")
PAIR = ("pair_0", "pair_1")
BLK_PAIR = ("blk_0", "blk_1", "blk_2", "pair_0", "pair_1")


def shifted(block, axis, distance):
    devices = range(lax.axis_size(axis))
    route = [((i - distance) % len(devices), i) for i in devices]
    return lax.ppermute(block, axis, route)


def per_device(
    particles,
    log_prior,
    transition,
    drive_vector,
    current,
    decay_rate,
    obs_matrix,
    obs_weight,
    observed,
    ancestors,
    cycle_pick,
    pair_pick,
):
    state = particles
    logw = log_prior
    rounded = state.astype(jnp.bfloat16)
    for step_index in range(STEPS):
        drift = (
            jnp.dot(rounded, transition, preferred_element_type=jnp.float32)
            + current[step_index] * drive_vector
        )
        state = decay_rate * state + jnp.tanh(drift)
        rounded = state.astype(jnp.bfloat16)
        predicted = jnp.dot(rounded, obs_matrix, preferred_element_type=jnp.float32)
        misfit = predicted - observed[step_index]
        logw = logw - 0.5 * jnp.sum(obs_weight * misfit * misfit, axis=1)
    n_blk = lax.axis_size(BLK)
    n_pair = lax.axis_size(PAIR)
    groups = n_blk * n_pair
    rows_here = state.shape[0]
    n_cycle = cycle_pick.shape[0]
    n_pairs = pair_pick.shape[0]

    local_peak = jnp.max(logw)
    expw = jnp.exp(logw - local_peak)
    local_sum = jnp.sum(expw)
    weighted = jnp.dot(expw, state, precision=lax.Precision.HIGHEST)
    width = state.shape[1]
    stamp = jnp.zeros((1, width), jnp.float32).at[0, 0].set(local_peak).at[0, 1].set(local_sum)

    cycle_in = shifted(jnp.concatenate([state[ancestors[cycle_pick]], stamp]), BLK, 1)
    pair_in = shifted(jnp.concatenate([state[ancestors[pair_pick]], stamp]), PAIR, n_pair // 2)

    packed = jnp.concatenate([local_peak[None], local_sum[None], weighted])
    for axis, size in ((PAIR, n_pair), (BLK, n_blk)):
        bit = 1
        while bit < size:
            other = lax.ppermute(packed, axis, [(i, i ^ bit) for i in range(size)])
            peak = jnp.maximum(packed[0], other[0])
            mine_scale = jnp.exp(packed[0] - peak)
            other_scale = jnp.exp(other[0] - peak)
            packed = jnp.concatenate([peak[None], packed[1:] * mine_scale + other[1:] * other_scale])
            bit *= 2
    peak = packed[0]
    total = packed[1]
    mean_state = packed[2:] / total

    def group_weight(device_peak, device_sum):
        return jnp.log(jnp.maximum(groups * (device_sum * jnp.exp(device_peak - peak)) / total, 0.1))

    own_w = group_weight(local_peak, local_sum)
    cycle_w = group_weight(cycle_in[n_cycle, 0], cycle_in[n_cycle, 1])
    pair_w = group_weight(pair_in[n_pairs, 0], pair_in[n_pairs, 1])

    source = (
        ancestors.at[cycle_pick]
        .set(rows_here + jnp.arange(n_cycle, dtype=jnp.int32))
        .at[pair_pick]
        .set(rows_here + n_cycle + jnp.arange(n_pairs, dtype=jnp.int32))
    )
    table = jnp.concatenate([state, cycle_in[:n_cycle], pair_in[:n_pairs]], axis=0)
    migrated = table[source]
    group_logw = jnp.where(
        source >= rows_here + n_cycle,
        pair_w,
        jnp.where(source >= rows_here, cycle_w, own_w),
    )
    return (migrated, group_logw, mean_state)


def solution(mesh):
    torus = Mesh(
        mesh.devices.reshape(2, 8, 2, 2, 4), ("blk_0", "blk_1", "blk_2", "pair_0", "pair_1")
    )
    in_specs = (
        P(BLK_PAIR, None),
        P(BLK_PAIR),
        P(),
        P(),
        P(),
        P(),
        P(),
        P(),
        P(),
        P(BLK_PAIR),
        P(BLK_PAIR),
        P(BLK_PAIR),
    )
    out_specs = (P(BLK_PAIR, None), P(BLK_PAIR), P())
    return jax.shard_map(
        per_device, mesh=torus, in_specs=in_specs, out_specs=out_specs, check_vma=False
    )
```

```python
import jax
import jax.numpy as jnp
from jax import lax
from jax.sharding import Mesh
from jax.sharding import PartitionSpec as P


STEPS = 4
BLK = ("blk_0", "blk_1", "blk_2")
PAIR = ("pair_0", "pair_1")
BLK_PAIR = ("blk_0", "blk_1", "blk_2", "pair_0", "pair_1")


def shifted(block, axis, distance):
    devices = range(lax.axis_size(axis))
    route = [((i - distance) % len(devices), i) for i in devices]
    return lax.ppermute(block, axis, route)


def window(
    particles,
    log_prior,
    transition,
    drive_vector,
    current,
    decay_rate,
    obs_matrix,
    obs_weight,
    observed,
    ancestors,
    cycle_pick,
    pair_pick,
):
    state = particles
    logw = log_prior
    rounded = state.astype(jnp.bfloat16)
    for step_index in range(STEPS):
        drift = (
            jnp.dot(rounded, transition, preferred_element_type=jnp.float32)
            + current[step_index] * drive_vector
        )
        state = decay_rate * state + jnp.tanh(drift)
        rounded = state.astype(jnp.bfloat16)
        predicted = jnp.dot(rounded, obs_matrix, preferred_element_type=jnp.float32)
        misfit = predicted - observed[step_index]
        logw = logw - 0.5 * jnp.sum(obs_weight * misfit * misfit, axis=1)
    n_blk = lax.axis_size(BLK)
    n_pair = lax.axis_size(PAIR)
    groups = n_blk * n_pair
    rows_here, width = state.shape
    n_cycle = cycle_pick.shape[0]
    n_pairs = pair_pick.shape[0]

    local_peak = jnp.max(logw)
    expw = jnp.exp(logw - local_peak)
    local_sum = jnp.sum(expw)
    weighted = jnp.dot(expw, state, precision=lax.Precision.HIGHEST)
    stamp = jnp.zeros((1, width), jnp.float32).at[0, 0].set(local_peak).at[0, 1].set(local_sum)

    cycle_in = shifted(jnp.concatenate([state[ancestors[cycle_pick]], stamp]), BLK, 1)
    pair_in = shifted(jnp.concatenate([state[ancestors[pair_pick]], stamp]), PAIR, n_pair // 2)

    lanes = 128
    k = width // lanes
    message = jnp.concatenate(
        [
            weighted.reshape(k, lanes),
            jnp.full((1, lanes), local_sum),
            jnp.full((1, lanes), local_peak),
            jnp.zeros((8 - (k + 2) % 8 if (k + 2) % 8 else 0, lanes), jnp.float32),
        ]
    )
    pad = message.shape[0] - (k + 2)
    for axis, size in ((PAIR, n_pair), (BLK, n_blk)):
        bit = 1
        while bit < size:
            other = lax.ppermute(message, axis, [(i, i ^ bit) for i in range(size)])
            peak_row = jnp.maximum(message[k + 1], other[k + 1])
            mine_scale = jnp.exp(message[k + 1] - peak_row)
            other_scale = jnp.exp(other[k + 1] - peak_row)
            body = message[: k + 1] * mine_scale + other[: k + 1] * other_scale
            message = jnp.concatenate([body, peak_row[None], jnp.zeros((pad, lanes), jnp.float32)])
            bit *= 2
    total = message[k, 0]
    peak = message[k + 1, 0]
    mean_state = message[:k].reshape(width) / total

    def group_weight(device_peak, device_sum):
        return jnp.log(jnp.maximum(groups * (device_sum * jnp.exp(device_peak - peak)) / total, 0.1))

    own_w = group_weight(local_peak, local_sum)
    cycle_w = group_weight(cycle_in[n_cycle, 0], cycle_in[n_cycle, 1])
    pair_w = group_weight(pair_in[n_pairs, 0], pair_in[n_pairs, 1])

    source = (
        ancestors.at[cycle_pick]
        .set(rows_here + jnp.arange(n_cycle, dtype=jnp.int32))
        .at[pair_pick]
        .set(rows_here + n_cycle + jnp.arange(n_pairs, dtype=jnp.int32))
    )
    table = jnp.concatenate([state, cycle_in[:n_cycle], pair_in[:n_pairs]], axis=0)
    migrated = table[source]
    group_logw = jnp.where(
        source >= rows_here + n_cycle,
        pair_w,
        jnp.where(source >= rows_here, cycle_w, own_w),
    )
    return (migrated, group_logw, mean_state)


def solution(mesh):
    torus = Mesh(
        mesh.devices.reshape(2, 8, 2, 2, 4), ("blk_0", "blk_1", "blk_2", "pair_0", "pair_1")
    )
    in_specs = (
        P(BLK_PAIR, None),
        P(BLK_PAIR),
        P(),
        P(),
        P(),
        P(),
        P(),
        P(),
        P(),
        P(BLK_PAIR),
        P(BLK_PAIR),
        P(BLK_PAIR),
    )
    out_specs = (P(BLK_PAIR, None), P(BLK_PAIR), P())
    return jax.shard_map(
        window, mesh=torus, in_specs=in_specs, out_specs=out_specs, check_vma=False
    )
```

```python
import jax
import jax.numpy as jnp
from jax import lax
from jax.experimental import pallas as pl
from jax.experimental.pallas import tpu as pltpu
from jax.sharding import Mesh
from jax.sharding import PartitionSpec as P


STEPS = 4
BLK = ("blk_0", "blk_1", "blk_2")
PAIR = ("pair_0", "pair_1")
BLK_PAIR = ("blk_0", "blk_1", "blk_2", "pair_0", "pair_1")


def shifted(block, axis, distance):
    devices = range(lax.axis_size(axis))
    route = [((i - distance) % len(devices), i) for i in devices]
    return lax.ppermute(block, axis, route)


def steps_kernel(
    current_ref, state_ref, prior_ref, transition_ref, drive_ref, decay_ref,
    obs_matrix_ref, obs_weight_ref, observed_ref, state_out, logw_out,
):
    state = state_ref[...]
    logw = prior_ref[...]
    drive = drive_ref[...]
    decay = decay_ref[...]
    obs_weight = obs_weight_ref[...]
    rounded = state.astype(jnp.bfloat16)
    for step_index in range(STEPS):
        drift = (
            jnp.dot(rounded, transition_ref[...], preferred_element_type=jnp.float32)
            + current_ref[step_index] * drive
        )
        state = decay * state + jnp.tanh(drift)
        rounded = state.astype(jnp.bfloat16)
        predicted = jnp.dot(rounded, obs_matrix_ref[...], preferred_element_type=jnp.float32)
        misfit = predicted - observed_ref[step_index : step_index + 1, :]
        logw = logw - 0.5 * jnp.sum(obs_weight * misfit * misfit, axis=1, keepdims=True)
    state_out[...] = state
    logw_out[...] = logw


def run_steps(particles, log_prior, transition, drive_vector, current, decay_rate, obs_matrix, obs_weight, observed):
    rows, width = particles.shape
    n_obs = obs_matrix.shape[1]
    block = 256
    whole = lambda i: (0, 0)
    state, logw = pl.pallas_call(
        steps_kernel,
        grid=(rows // block,),
        in_specs=[
            pl.BlockSpec(memory_space=pltpu.SMEM),
            pl.BlockSpec((block, width), lambda i: (i, 0)),
            pl.BlockSpec((block, 1), lambda i: (i, 0)),
            pl.BlockSpec((width, width), whole),
            pl.BlockSpec((1, width), whole),
            pl.BlockSpec((1, width), whole),
            pl.BlockSpec((width, n_obs), whole),
            pl.BlockSpec((1, n_obs), whole),
            pl.BlockSpec(observed.shape, whole),
        ],
        out_specs=[
            pl.BlockSpec((block, width), lambda i: (i, 0)),
            pl.BlockSpec((block, 1), lambda i: (i, 0)),
        ],
        out_shape=[
            jax.ShapeDtypeStruct((rows, width), jnp.float32),
            jax.ShapeDtypeStruct((rows, 1), jnp.float32),
        ],
        compiler_params=pltpu.CompilerParams(dimension_semantics=("arbitrary",)),
        cost_estimate=pl.CostEstimate(
            flops=2 * STEPS * rows * width * (width + n_obs),
            transcendentals=STEPS * rows * width,
            bytes_accessed=2 * rows * width * 4 + width * width * 2,
        ),
    )(
        current,
        particles,
        log_prior.reshape(rows, 1),
        transition,
        drive_vector.reshape(1, width),
        decay_rate.reshape(1, width),
        obs_matrix,
        obs_weight.reshape(1, n_obs),
        observed,
    )
    return state, logw.reshape(rows)


def window(
    particles,
    log_prior,
    transition,
    drive_vector,
    current,
    decay_rate,
    obs_matrix,
    obs_weight,
    observed,
    ancestors,
    cycle_pick,
    pair_pick,
):
    state, logw = run_steps(
        particles, log_prior, transition, drive_vector, current, decay_rate, obs_matrix, obs_weight, observed
    )
    n_blk = lax.axis_size(BLK)
    n_pair = lax.axis_size(PAIR)
    groups = n_blk * n_pair
    rows_here, width = state.shape
    n_cycle = cycle_pick.shape[0]
    n_pairs = pair_pick.shape[0]

    local_peak = jnp.max(logw)
    expw = jnp.exp(logw - local_peak)
    local_sum = jnp.sum(expw)
    weighted = jnp.dot(expw, state, precision=lax.Precision.HIGHEST)
    stamp = jnp.zeros((1, width), jnp.float32).at[0, 0].set(local_peak).at[0, 1].set(local_sum)

    cycle_in = shifted(jnp.concatenate([state[ancestors[cycle_pick]], stamp]), BLK, 1)
    pair_in = shifted(jnp.concatenate([state[ancestors[pair_pick]], stamp]), PAIR, n_pair // 2)

    lanes = 128
    k = width // lanes
    message = jnp.concatenate(
        [
            weighted.reshape(k, lanes),
            jnp.full((1, lanes), local_sum),
            jnp.full((1, lanes), local_peak),
            jnp.zeros((8 - (k + 2) % 8 if (k + 2) % 8 else 0, lanes), jnp.float32),
        ]
    )
    pad = message.shape[0] - (k + 2)
    for axis, size in ((PAIR, n_pair), (BLK, n_blk)):
        bit = 1
        while bit < size:
            other = lax.ppermute(message, axis, [(i, i ^ bit) for i in range(size)])
            peak_row = jnp.maximum(message[k + 1], other[k + 1])
            mine_scale = jnp.exp(message[k + 1] - peak_row)
            other_scale = jnp.exp(other[k + 1] - peak_row)
            body = message[: k + 1] * mine_scale + other[: k + 1] * other_scale
            message = jnp.concatenate([body, peak_row[None], jnp.zeros((pad, lanes), jnp.float32)])
            bit *= 2
    total = message[k, 0]
    peak = message[k + 1, 0]
    mean_state = message[:k].reshape(width) / total

    def group_weight(device_peak, device_sum):
        return jnp.log(jnp.maximum(groups * (device_sum * jnp.exp(device_peak - peak)) / total, 0.1))

    own_w = group_weight(local_peak, local_sum)
    cycle_w = group_weight(cycle_in[n_cycle, 0], cycle_in[n_cycle, 1])
    pair_w = group_weight(pair_in[n_pairs, 0], pair_in[n_pairs, 1])

    source = (
        ancestors.at[cycle_pick]
        .set(rows_here + jnp.arange(n_cycle, dtype=jnp.int32))
        .at[pair_pick]
        .set(rows_here + n_cycle + jnp.arange(n_pairs, dtype=jnp.int32))
    )
    table = jnp.concatenate([state, cycle_in[:n_cycle], pair_in[:n_pairs]], axis=0)
    migrated = table[source]
    group_logw = jnp.where(
        source >= rows_here + n_cycle,
        pair_w,
        jnp.where(source >= rows_here, cycle_w, own_w),
    )
    return (migrated, group_logw, mean_state)


def solution(mesh):
    torus = Mesh(
        mesh.devices.reshape(2, 8, 2, 2, 4), ("blk_0", "blk_1", "blk_2", "pair_0", "pair_1")
    )
    in_specs = (
        P(BLK_PAIR, None),
        P(BLK_PAIR),
        P(),
        P(),
        P(),
        P(),
        P(),
        P(),
        P(),
        P(BLK_PAIR),
        P(BLK_PAIR),
        P(BLK_PAIR),
    )
    out_specs = (P(BLK_PAIR, None), P(BLK_PAIR), P())
    return jax.shard_map(
        window, mesh=torus, in_specs=in_specs, out_specs=out_specs, check_vma=False
    )
```

```python
import jax
import jax.numpy as jnp
from jax import lax
from jax.experimental import pallas as pl
from jax.experimental.pallas import tpu as pltpu
from jax.sharding import Mesh
from jax.sharding import PartitionSpec as P


STEPS = 4
BLK = ("blk_0", "blk_1", "blk_2")
PAIR = ("pair_0", "pair_1")
BLK_PAIR = ("blk_0", "blk_1", "blk_2", "pair_0", "pair_1")


def shifted(block, axis, distance):
    devices = range(lax.axis_size(axis))
    route = [((i - distance) % len(devices), i) for i in devices]
    return lax.ppermute(block, axis, route)


def steps_kernel(
    current_ref, state_ref, prior_ref, transition_ref, drive_ref, decay_ref,
    obs_matrix_ref, obs_weight_ref, observed_ref, state_out, message_out,
    peak_acc, sum_acc, weighted_acc,
):
    block = pl.program_id(0)
    state = state_ref[...]
    logw = prior_ref[...]
    drive = drive_ref[...]
    decay = decay_ref[...]
    obs_weight = obs_weight_ref[...]
    rounded = state.astype(jnp.bfloat16)
    for step_index in range(STEPS):
        drift = (
            jnp.dot(rounded, transition_ref[...], preferred_element_type=jnp.float32)
            + current_ref[step_index] * drive
        )
        state = decay * state + jnp.tanh(drift)
        rounded = state.astype(jnp.bfloat16)
        predicted = jnp.dot(rounded, obs_matrix_ref[...], preferred_element_type=jnp.float32)
        misfit = predicted - observed_ref[step_index : step_index + 1, :]
        logw = logw - 0.5 * jnp.sum(obs_weight * misfit * misfit, axis=1, keepdims=True)
    state_out[...] = state

    @pl.when(block == 0)
    def _():
        peak_acc[...] = jnp.full(peak_acc.shape, -jnp.inf, jnp.float32)
        sum_acc[...] = jnp.zeros(sum_acc.shape, jnp.float32)
        weighted_acc[...] = jnp.zeros(weighted_acc.shape, jnp.float32)

    old_peak = peak_acc[...]
    new_peak = jnp.maximum(old_peak, jnp.max(logw, axis=0, keepdims=True))
    scale = jnp.exp(old_peak - new_peak)
    expw = jnp.exp(logw - new_peak[:, :1])
    sum_acc[...] = sum_acc[...] * scale + jnp.sum(expw, axis=0, keepdims=True)
    weighted_acc[...] = weighted_acc[...] * scale[:, :1] + jnp.sum(expw * state, axis=0, keepdims=True)
    peak_acc[...] = new_peak

    @pl.when(block == pl.num_programs(0) - 1)
    def _():
        lanes = peak_acc.shape[1]
        k = weighted_acc.shape[1] // lanes
        for row in range(k):
            message_out[row : row + 1, :] = weighted_acc[:, row * lanes : (row + 1) * lanes]
        message_out[k : k + 1, :] = sum_acc[...]
        message_out[k + 1 : k + 2, :] = peak_acc[...]
        rest = message_out.shape[0] - (k + 2)
        if rest:
            message_out[k + 2 :, :] = jnp.zeros((rest, lanes), jnp.float32)


def run_steps(particles, log_prior, transition, drive_vector, current, decay_rate, obs_matrix, obs_weight, observed):
    rows, width = particles.shape
    n_obs = obs_matrix.shape[1]
    block = 256
    lanes = 128
    k = width // lanes
    message_rows = max(-(-(k + 2) // 8) * 8, 2 * k)
    whole = lambda i: (0, 0)
    return pl.pallas_call(
        steps_kernel,
        grid=(rows // block,),
        in_specs=[
            pl.BlockSpec(memory_space=pltpu.SMEM),
            pl.BlockSpec((block, width), lambda i: (i, 0)),
            pl.BlockSpec((block, 1), lambda i: (i, 0)),
            pl.BlockSpec((width, width), whole),
            pl.BlockSpec((1, width), whole),
            pl.BlockSpec((1, width), whole),
            pl.BlockSpec((width, n_obs), whole),
            pl.BlockSpec((1, n_obs), whole),
            pl.BlockSpec(observed.shape, whole),
        ],
        out_specs=[
            pl.BlockSpec((block, width), lambda i: (i, 0)),
            pl.BlockSpec((message_rows, lanes), whole),
        ],
        out_shape=[
            jax.ShapeDtypeStruct((rows, width), jnp.float32),
            jax.ShapeDtypeStruct((message_rows, lanes), jnp.float32),
        ],
        scratch_shapes=[
            pltpu.VMEM((1, lanes), jnp.float32),
            pltpu.VMEM((1, lanes), jnp.float32),
            pltpu.VMEM((1, width), jnp.float32),
        ],
        compiler_params=pltpu.CompilerParams(dimension_semantics=("arbitrary",)),
        cost_estimate=pl.CostEstimate(
            flops=2 * STEPS * rows * width * (width + n_obs),
            transcendentals=STEPS * rows * width,
            bytes_accessed=2 * rows * width * 4 + width * width * 2,
        ),
    )(
        current,
        particles,
        log_prior.reshape(rows, 1),
        transition,
        drive_vector.reshape(1, width),
        decay_rate.reshape(1, width),
        obs_matrix,
        obs_weight.reshape(1, n_obs),
        observed,
    )


def window(
    particles,
    log_prior,
    transition,
    drive_vector,
    current,
    decay_rate,
    obs_matrix,
    obs_weight,
    observed,
    ancestors,
    cycle_pick,
    pair_pick,
):
    state, message = run_steps(
        particles, log_prior, transition, drive_vector, current, decay_rate, obs_matrix, obs_weight, observed
    )
    n_blk = lax.axis_size(BLK)
    n_pair = lax.axis_size(PAIR)
    groups = n_blk * n_pair
    rows_here, width = state.shape
    n_cycle = cycle_pick.shape[0]
    n_pairs = pair_pick.shape[0]
    lanes = message.shape[1]
    k = width // lanes
    local_sum = message[k, 0]
    local_peak = message[k + 1, 0]
    stamp = message[k : 2 * k].reshape(1, width)

    cycle_in = shifted(jnp.concatenate([state[ancestors[cycle_pick]], stamp]), BLK, 1)
    pair_in = shifted(jnp.concatenate([state[ancestors[pair_pick]], stamp]), PAIR, n_pair // 2)

    pad = message.shape[0] - (k + 2)
    for axis, size in ((PAIR, n_pair), (BLK, n_blk)):
        bit = 1
        while bit < size:
            other = lax.ppermute(message, axis, [(i, i ^ bit) for i in range(size)])
            peak_row = jnp.maximum(message[k + 1], other[k + 1])
            mine_scale = jnp.exp(message[k + 1] - peak_row)
            other_scale = jnp.exp(other[k + 1] - peak_row)
            body = message[: k + 1] * mine_scale + other[: k + 1] * other_scale
            message = jnp.concatenate([body, peak_row[None], jnp.zeros((pad, lanes), jnp.float32)])
            bit *= 2
    total = message[k, 0]
    peak = message[k + 1, 0]
    mean_state = message[:k].reshape(width) / total

    def group_weight(device_peak, device_sum):
        return jnp.log(jnp.maximum(groups * (device_sum * jnp.exp(device_peak - peak)) / total, 0.1))

    own_w = group_weight(local_peak, local_sum)
    cycle_w = group_weight(cycle_in[n_cycle, lanes], cycle_in[n_cycle, 0])
    pair_w = group_weight(pair_in[n_pairs, lanes], pair_in[n_pairs, 0])

    source = (
        ancestors.at[cycle_pick]
        .set(rows_here + jnp.arange(n_cycle, dtype=jnp.int32))
        .at[pair_pick]
        .set(rows_here + n_cycle + jnp.arange(n_pairs, dtype=jnp.int32))
    )
    table = jnp.concatenate([state, cycle_in[:n_cycle], pair_in[:n_pairs]], axis=0)
    migrated = table[source]
    group_logw = jnp.where(
        source >= rows_here + n_cycle,
        pair_w,
        jnp.where(source >= rows_here, cycle_w, own_w),
    )
    return (migrated, group_logw, mean_state)


def solution(mesh):
    torus = Mesh(
        mesh.devices.reshape(2, 8, 2, 2, 4), ("blk_0", "blk_1", "blk_2", "pair_0", "pair_1")
    )
    in_specs = (
        P(BLK_PAIR, None),
        P(BLK_PAIR),
        P(),
        P(),
        P(),
        P(),
        P(),
        P(),
        P(),
        P(BLK_PAIR),
        P(BLK_PAIR),
        P(BLK_PAIR),
    )
    out_specs = (P(BLK_PAIR, None), P(BLK_PAIR), P())
    return jax.shard_map(
        window, mesh=torus, in_specs=in_specs, out_specs=out_specs, check_vma=False
    )
```

```python
import jax
import jax.numpy as jnp
from jax import lax
from jax.experimental import pallas as pl
from jax.experimental.pallas import tpu as pltpu
from jax.sharding import Mesh
from jax.sharding import PartitionSpec as P


STEPS = 4
BLK = ("blk_0", "blk_1", "blk_2")
PAIR = ("pair_0", "pair_1")
BLK_PAIR = ("blk_0", "blk_1", "blk_2", "pair_0", "pair_1")


def shifted(block, axis, distance):
    devices = range(lax.axis_size(axis))
    route = [((i - distance) % len(devices), i) for i in devices]
    return lax.ppermute(block, axis, route)


def steps_kernel(
    current_ref, state_ref, prior_ref, transition_ref, drive_ref, decay_ref,
    obs_matrix_ref, obs_weight_ref, observed_ref, state_out, message_out,
    peak_acc, sum_acc, weighted_acc,
):
    block = pl.program_id(0)
    state = state_ref[...]
    logw = prior_ref[...]
    drive = drive_ref[...]
    decay = decay_ref[...]
    obs_weight = obs_weight_ref[...]
    rounded = state.astype(jnp.bfloat16)
    for step_index in range(STEPS):
        drift = (
            jnp.dot(rounded, transition_ref[...], preferred_element_type=jnp.float32)
            + current_ref[step_index] * drive
        )
        state = decay * state + jnp.tanh(drift)
        rounded = state.astype(jnp.bfloat16)
        predicted = jnp.dot(rounded, obs_matrix_ref[...], preferred_element_type=jnp.float32)
        misfit = predicted - observed_ref[step_index : step_index + 1, :]
        logw = logw - 0.5 * jnp.sum(obs_weight * misfit * misfit, axis=1, keepdims=True)
    state_out[...] = state

    @pl.when(block == 0)
    def _():
        peak_acc[...] = jnp.full(peak_acc.shape, -jnp.inf, jnp.float32)
        sum_acc[...] = jnp.zeros(sum_acc.shape, jnp.float32)
        weighted_acc[...] = jnp.zeros(weighted_acc.shape, jnp.float32)

    old_peak = peak_acc[...]
    new_peak = jnp.maximum(old_peak, jnp.max(logw, axis=0, keepdims=True))
    scale = jnp.exp(old_peak - new_peak)
    expw = jnp.exp(logw - new_peak[:, :1])
    sum_acc[...] = sum_acc[...] * scale + jnp.sum(expw, axis=0, keepdims=True)
    weighted_acc[...] = weighted_acc[...] * scale[:, :1] + jnp.sum(expw * state, axis=0, keepdims=True)
    peak_acc[...] = new_peak

    @pl.when(block == pl.num_programs(0) - 1)
    def _():
        lanes = peak_acc.shape[1]
        k = weighted_acc.shape[1] // lanes
        for row in range(k):
            message_out[row : row + 1, :] = weighted_acc[:, row * lanes : (row + 1) * lanes]
        message_out[k : k + 1, :] = sum_acc[...]
        message_out[k + 1 : k + 2, :] = peak_acc[...]
        rest = message_out.shape[0] - (k + 2)
        if rest:
            message_out[k + 2 :, :] = jnp.zeros((rest, lanes), jnp.float32)


def run_steps(particles, log_prior, transition, drive_vector, current, decay_rate, obs_matrix, obs_weight, observed):
    rows, width = particles.shape
    n_obs = obs_matrix.shape[1]
    block = 256
    lanes = 128
    k = width // lanes
    message_rows = max(-(-(k + 2) // 8) * 8, 2 * k)
    whole = lambda i: (0, 0)
    return pl.pallas_call(
        steps_kernel,
        grid=(rows // block,),
        in_specs=[
            pl.BlockSpec(memory_space=pltpu.SMEM),
            pl.BlockSpec((block, width), lambda i: (i, 0)),
            pl.BlockSpec((block, 1), lambda i: (i, 0)),
            pl.BlockSpec((width, width), whole),
            pl.BlockSpec((1, width), whole),
            pl.BlockSpec((1, width), whole),
            pl.BlockSpec((width, n_obs), whole),
            pl.BlockSpec((1, n_obs), whole),
            pl.BlockSpec(observed.shape, whole),
        ],
        out_specs=[
            pl.BlockSpec((block, width), lambda i: (i, 0)),
            pl.BlockSpec((message_rows, lanes), whole),
        ],
        out_shape=[
            jax.ShapeDtypeStruct((rows, width), jnp.float32),
            jax.ShapeDtypeStruct((message_rows, lanes), jnp.float32),
        ],
        scratch_shapes=[
            pltpu.VMEM((1, lanes), jnp.float32),
            pltpu.VMEM((1, lanes), jnp.float32),
            pltpu.VMEM((1, width), jnp.float32),
        ],
        compiler_params=pltpu.CompilerParams(dimension_semantics=("arbitrary",)),
        cost_estimate=pl.CostEstimate(
            flops=2 * STEPS * rows * width * (width + n_obs),
            transcendentals=STEPS * rows * width,
            bytes_accessed=2 * rows * width * 4 + width * width * 2,
        ),
    )(
        current,
        particles,
        log_prior.reshape(rows, 1),
        transition,
        drive_vector.reshape(1, width),
        decay_rate.reshape(1, width),
        obs_matrix,
        obs_weight.reshape(1, n_obs),
        observed,
    )


def window(
    particles,
    log_prior,
    transition,
    drive_vector,
    current,
    decay_rate,
    obs_matrix,
    obs_weight,
    observed,
    ancestors,
    cycle_pick,
    pair_pick,
):
    state, message = run_steps(
        particles, log_prior, transition, drive_vector, current, decay_rate, obs_matrix, obs_weight, observed
    )
    n_blk = lax.axis_size(BLK)
    n_pair = lax.axis_size(PAIR)
    groups = n_blk * n_pair
    rows_here, width = state.shape
    n_cycle = cycle_pick.shape[0]
    n_pairs = pair_pick.shape[0]
    lanes = message.shape[1]
    k = width // lanes
    local_sum = message[k, 0]
    local_peak = message[k + 1, 0]
    stamp = message[k : 2 * k].reshape(1, width)

    cycle_out = jnp.concatenate([state[ancestors[cycle_pick]], stamp])
    pair_out = jnp.concatenate([state[ancestors[pair_pick]], stamp])
    cycle_in = shifted(cycle_out, BLK, 1)
    pair_in = shifted(pair_out, PAIR, n_pair // 2)

    pad = message.shape[0] - (k + 2)
    for axis, size in ((PAIR, n_pair), (BLK, n_blk)):
        bit = 1
        while bit < size:
            other = lax.ppermute(message, axis, [(i, i ^ bit) for i in range(size)])
            peak_row = jnp.maximum(message[k + 1], other[k + 1])
            mine_scale = jnp.exp(message[k + 1] - peak_row)
            other_scale = jnp.exp(other[k + 1] - peak_row)
            body = message[: k + 1] * mine_scale + other[: k + 1] * other_scale
            message = jnp.concatenate([body, peak_row[None], jnp.zeros((pad, lanes), jnp.float32)])
            bit *= 2
    total = message[k, 0]
    peak = message[k + 1, 0]
    mean_state = message[:k].reshape(width) / total

    def group_weight(device_peak, device_sum):
        return jnp.log(jnp.maximum(groups * (device_sum * jnp.exp(device_peak - peak)) / total, 0.1))

    own_w = group_weight(local_peak, local_sum)
    cycle_w = group_weight(cycle_in[n_cycle, lanes], cycle_in[n_cycle, 0])
    pair_w = group_weight(pair_in[n_pairs, lanes], pair_in[n_pairs, 0])

    source = (
        ancestors.at[cycle_pick]
        .set(rows_here + jnp.arange(n_cycle, dtype=jnp.int32))
        .at[pair_pick]
        .set(rows_here + n_cycle + jnp.arange(n_pairs, dtype=jnp.int32))
    )
    table = jnp.concatenate([state, cycle_in[:n_cycle], pair_in[:n_pairs]], axis=0)
    migrated = table[source]
    group_logw = jnp.where(
        source >= rows_here + n_cycle,
        pair_w,
        jnp.where(source >= rows_here, cycle_w, own_w),
    )
    return (migrated, group_logw, mean_state)


def solution(mesh):
    torus = Mesh(
        mesh.devices.reshape(2, 8, 2, 2, 4), ("blk_0", "blk_1", "blk_2", "pair_0", "pair_1")
    )
    in_specs = (
        P(BLK_PAIR, None),
        P(BLK_PAIR),
        P(),
        P(),
        P(),
        P(),
        P(),
        P(),
        P(),
        P(BLK_PAIR),
        P(BLK_PAIR),
        P(BLK_PAIR),
    )
    out_specs = (P(BLK_PAIR, None), P(BLK_PAIR), P())
    return jax.shard_map(
        window, mesh=torus, in_specs=in_specs, out_specs=out_specs, check_vma=False
    )
```

```python
import jax
import jax.numpy as jnp
from jax import lax
from jax.experimental import pallas as pl
from jax.experimental.pallas import tpu as pltpu
from jax.sharding import Mesh
from jax.sharding import PartitionSpec as P


STEPS = 4
BLK = ("blk_0", "blk_1", "blk_2")
PAIR = ("pair_0", "pair_1")
BLK_PAIR = ("blk_0", "blk_1", "blk_2", "pair_0", "pair_1")


def shifted(block, axis, distance):
    devices = range(lax.axis_size(axis))
    route = [((i - distance) % len(devices), i) for i in devices]
    return lax.ppermute(block, axis, route)


def steps_kernel(
    current_ref, state_ref, prior_ref, transition_ref, drive_ref, decay_ref,
    obs_matrix_ref, obs_weight_ref, observed_ref, state_out, message_out,
    peak_acc, sum_acc, weighted_acc,
):
    block = pl.program_id(0)
    state = state_ref[...]
    logw = prior_ref[...]
    drive = drive_ref[...]
    decay = decay_ref[...]
    obs_weight = obs_weight_ref[...]
    rounded = state.astype(jnp.bfloat16)
    for step_index in range(STEPS):
        drift = (
            jnp.dot(rounded, transition_ref[...], preferred_element_type=jnp.float32)
            + current_ref[step_index] * drive
        )
        state = decay * state + jnp.tanh(drift)
        rounded = state.astype(jnp.bfloat16)
        predicted = jnp.dot(rounded, obs_matrix_ref[...], preferred_element_type=jnp.float32)
        misfit = predicted - observed_ref[step_index : step_index + 1, :]
        logw = logw - 0.5 * jnp.sum(obs_weight * misfit * misfit, axis=1, keepdims=True)
    state_out[...] = state

    @pl.when(block == 0)
    def _():
        peak_acc[...] = jnp.full(peak_acc.shape, -jnp.inf, jnp.float32)
        sum_acc[...] = jnp.zeros(sum_acc.shape, jnp.float32)
        weighted_acc[...] = jnp.zeros(weighted_acc.shape, jnp.float32)

    old_peak = peak_acc[...]
    new_peak = jnp.maximum(old_peak, jnp.max(logw, axis=0, keepdims=True))
    scale = jnp.exp(old_peak - new_peak)
    expw = jnp.exp(logw - new_peak[:, :1])
    sum_acc[...] = sum_acc[...] * scale + jnp.sum(expw, axis=0, keepdims=True)
    weighted_acc[...] = weighted_acc[...] * scale[:, :1] + jnp.sum(expw * state, axis=0, keepdims=True)
    peak_acc[...] = new_peak

    @pl.when(block == pl.num_programs(0) - 1)
    def _():
        lanes = peak_acc.shape[1]
        k = weighted_acc.shape[1] // lanes
        for row in range(k):
            message_out[row : row + 1, :] = weighted_acc[:, row * lanes : (row + 1) * lanes]
        message_out[k : k + 1, :] = sum_acc[...]
        message_out[k + 1 : k + 2, :] = peak_acc[...]
        rest = message_out.shape[0] - (k + 2)
        if rest:
            message_out[k + 2 :, :] = jnp.zeros((rest, lanes), jnp.float32)


def run_steps(particles, log_prior, transition, drive_vector, current, decay_rate, obs_matrix, obs_weight, observed):
    rows, width = particles.shape
    n_obs = obs_matrix.shape[1]
    block = 256
    lanes = 128
    k = width // lanes
    message_rows = max(-(-(k + 2) // 8) * 8, 2 * k)
    whole = lambda i: (0, 0)
    return pl.pallas_call(
        steps_kernel,
        grid=(rows // block,),
        in_specs=[
            pl.BlockSpec(memory_space=pltpu.SMEM),
            pl.BlockSpec((block, width), lambda i: (i, 0)),
            pl.BlockSpec((block, 1), lambda i: (i, 0)),
            pl.BlockSpec((width, width), whole),
            pl.BlockSpec((1, width), whole),
            pl.BlockSpec((1, width), whole),
            pl.BlockSpec((width, n_obs), whole),
            pl.BlockSpec((1, n_obs), whole),
            pl.BlockSpec(observed.shape, whole),
        ],
        out_specs=[
            pl.BlockSpec((block, width), lambda i: (i, 0)),
            pl.BlockSpec((message_rows, lanes), whole),
        ],
        out_shape=[
            jax.ShapeDtypeStruct((rows, width), jnp.float32),
            jax.ShapeDtypeStruct((message_rows, lanes), jnp.float32),
        ],
        scratch_shapes=[
            pltpu.VMEM((1, lanes), jnp.float32),
            pltpu.VMEM((1, lanes), jnp.float32),
            pltpu.VMEM((1, width), jnp.float32),
        ],
        compiler_params=pltpu.CompilerParams(dimension_semantics=("arbitrary",)),
        cost_estimate=pl.CostEstimate(
            flops=2 * STEPS * rows * width * (width + n_obs),
            transcendentals=STEPS * rows * width,
            bytes_accessed=2 * rows * width * 4 + width * width * 2,
        ),
    )(
        current,
        particles,
        log_prior.reshape(rows, 1),
        transition,
        drive_vector.reshape(1, width),
        decay_rate.reshape(1, width),
        obs_matrix,
        obs_weight.reshape(1, n_obs),
        observed,
    )


def pick_rows_kernel(ancestors_ref, pick_ref, state_hbm, stamp_ref, rows_out, sem):
    count = pick_ref.shape[0]

    def issue(i, carry):
        row = ancestors_ref[pick_ref[i]]
        pltpu.make_async_copy(state_hbm.at[pl.ds(row, 1)], rows_out.at[pl.ds(i, 1)], sem.at[0]).start()
        return carry

    lax.fori_loop(0, count, issue, 0)
    pltpu.make_async_copy(state_hbm.at[pl.ds(0, count)], rows_out.at[pl.ds(0, count)], sem.at[0]).wait()
    rows_out[count : count + 1, :] = stamp_ref[...]


def pick_rows(state, ancestors, pick, stamp):
    _, width = state.shape
    count = pick.shape[0]
    return pl.pallas_call(
        pick_rows_kernel,
        in_specs=[
            pl.BlockSpec(memory_space=pltpu.SMEM),
            pl.BlockSpec(memory_space=pltpu.SMEM),
            pl.BlockSpec(memory_space=pl.ANY),
            pl.BlockSpec(memory_space=pltpu.VMEM),
        ],
        out_specs=pl.BlockSpec(memory_space=pltpu.VMEM),
        out_shape=jax.ShapeDtypeStruct((count + 1, width), jnp.float32),
        scratch_shapes=[pltpu.SemaphoreType.DMA((1,))],
        cost_estimate=pl.CostEstimate(flops=0, transcendentals=0, bytes_accessed=2 * count * width * 4),
    )(ancestors, pick, state, stamp)


def assemble_kernel(
    ancestors_ref, cycle_pick_ref, pair_pick_ref, state_hbm, cycle_hbm, pair_hbm, migrated_out, sem
):
    rows = ancestors_ref.shape[0]
    n_cycle = cycle_pick_ref.shape[0]
    n_pairs = pair_pick_ref.shape[0]

    def resample(i, carry):
        row = ancestors_ref[i]
        pltpu.make_async_copy(state_hbm.at[pl.ds(row, 1)], migrated_out.at[pl.ds(i, 1)], sem.at[0]).start()
        return carry

    lax.fori_loop(0, rows, resample, 0)
    pltpu.make_async_copy(state_hbm, migrated_out, sem.at[0]).wait()

    def arrive_cycle(j, carry):
        row = cycle_pick_ref[j]
        pltpu.make_async_copy(cycle_hbm.at[pl.ds(j, 1)], migrated_out.at[pl.ds(row, 1)], sem.at[1]).start()
        return carry

    def arrive_pair(j, carry):
        row = pair_pick_ref[j]
        pltpu.make_async_copy(pair_hbm.at[pl.ds(j, 1)], migrated_out.at[pl.ds(row, 1)], sem.at[1]).start()
        return carry

    lax.fori_loop(0, n_cycle, arrive_cycle, 0)
    lax.fori_loop(0, n_pairs, arrive_pair, 0)
    pltpu.make_async_copy(cycle_hbm.at[pl.ds(0, n_cycle)], migrated_out.at[pl.ds(0, n_cycle)], sem.at[1]).wait()
    pltpu.make_async_copy(pair_hbm.at[pl.ds(0, n_pairs)], migrated_out.at[pl.ds(0, n_pairs)], sem.at[1]).wait()


def assemble(state, ancestors, cycle_pick, pair_pick, cycle_in, pair_in):
    rows, width = state.shape
    return pl.pallas_call(
        assemble_kernel,
        in_specs=[pl.BlockSpec(memory_space=pltpu.SMEM)] * 3 + [pl.BlockSpec(memory_space=pl.ANY)] * 3,
        out_specs=pl.BlockSpec(memory_space=pltpu.VMEM),
        out_shape=jax.ShapeDtypeStruct((rows, width), jnp.float32),
        scratch_shapes=[pltpu.SemaphoreType.DMA((2,))],
        cost_estimate=pl.CostEstimate(flops=0, transcendentals=0, bytes_accessed=4 * rows * width * 4),
    )(ancestors, cycle_pick, pair_pick, state, cycle_in, pair_in)


def window(
    particles,
    log_prior,
    transition,
    drive_vector,
    current,
    decay_rate,
    obs_matrix,
    obs_weight,
    observed,
    ancestors,
    cycle_pick,
    pair_pick,
):
    state, message = run_steps(
        particles, log_prior, transition, drive_vector, current, decay_rate, obs_matrix, obs_weight, observed
    )
    n_blk = lax.axis_size(BLK)
    n_pair = lax.axis_size(PAIR)
    groups = n_blk * n_pair
    rows_here, width = state.shape
    n_cycle = cycle_pick.shape[0]
    n_pairs = pair_pick.shape[0]
    lanes = message.shape[1]
    k = width // lanes
    stamp = message[k : 2 * k].reshape(1, width)

    cycle_out = pick_rows(state, ancestors, cycle_pick, stamp)
    pair_out = pick_rows(state, ancestors, pair_pick, stamp)
    cycle_in = shifted(cycle_out, BLK, 1)
    pair_in = shifted(pair_out, PAIR, n_pair // 2)

    pad = message.shape[0] - (k + 2)
    for axis, size in ((PAIR, n_pair), (BLK, n_blk)):
        bit = 1
        while bit < size:
            other = lax.ppermute(message, axis, [(i, i ^ bit) for i in range(size)])
            peak_row = jnp.maximum(message[k + 1], other[k + 1])
            mine_scale = jnp.exp(message[k + 1] - peak_row)
            other_scale = jnp.exp(other[k + 1] - peak_row)
            body = message[: k + 1] * mine_scale + other[: k + 1] * other_scale
            message = jnp.concatenate([body, peak_row[None], jnp.zeros((pad, lanes), jnp.float32)])
            bit *= 2
    total = message[k : k + 1]
    peak = message[k + 1 : k + 2]
    mean_state = (message[:k] / total).reshape(width)

    def group_weight(row):
        device_sum = row[:, :lanes]
        device_peak = row[:, lanes : 2 * lanes]
        return jnp.log(jnp.maximum(groups * (device_sum * jnp.exp(device_peak - peak)) / total, 0.1))

    own_w = group_weight(stamp)
    cycle_w = group_weight(cycle_in[n_cycle : n_cycle + 1])
    pair_w = group_weight(pair_in[n_pairs : n_pairs + 1])

    migrated = assemble(state, ancestors, cycle_pick, pair_pick, cycle_in, pair_in)
    source = (
        ancestors.at[cycle_pick]
        .set(rows_here + jnp.arange(n_cycle, dtype=jnp.int32))
        .at[pair_pick]
        .set(rows_here + n_cycle + jnp.arange(n_pairs, dtype=jnp.int32))
    )
    tiles = source.reshape(rows_here // lanes, lanes)
    group_logw = jnp.where(
        tiles >= rows_here + n_cycle,
        pair_w,
        jnp.where(tiles >= rows_here, cycle_w, own_w),
    ).reshape(rows_here)
    return (migrated, group_logw, mean_state)


def solution(mesh):
    torus = Mesh(
        mesh.devices.reshape(2, 8, 2, 2, 4), ("blk_0", "blk_1", "blk_2", "pair_0", "pair_1")
    )
    in_specs = (
        P(BLK_PAIR, None),
        P(BLK_PAIR),
        P(),
        P(),
        P(),
        P(),
        P(),
        P(),
        P(),
        P(BLK_PAIR),
        P(BLK_PAIR),
        P(BLK_PAIR),
    )
    out_specs = (P(BLK_PAIR, None), P(BLK_PAIR), P())
    return jax.shard_map(window, mesh=torus, in_specs=in_specs, out_specs=out_specs, check_vma=False)
```

```python
import jax
import jax.numpy as jnp
from jax import lax
from jax.experimental import pallas as pl
from jax.experimental.pallas import tpu as pltpu
from jax.sharding import Mesh
from jax.sharding import PartitionSpec as P


STEPS = 4
BLK = ("blk_0", "blk_1", "blk_2")
PAIR = ("pair_0", "pair_1")
BLK_PAIR = ("blk_0", "blk_1", "blk_2", "pair_0", "pair_1")


def shifted(block, axis, distance):
    devices = range(lax.axis_size(axis))
    route = [((i - distance) % len(devices), i) for i in devices]
    return lax.ppermute(block, axis, route)


def steps_kernel(
    current_ref, ancestors_ref, cycle_pick_ref, pair_pick_ref, state_ref, prior_ref, transition_ref,
    drive_ref, decay_ref, obs_matrix_ref, obs_weight_ref, observed_ref,
    state_out, message_out, cycle_out, pair_out,
    peak_acc, sum_acc, weighted_acc, full_state,
):
    block = pl.program_id(0)
    state = state_ref[...]
    logw = prior_ref[...]
    drive = drive_ref[...]
    decay = decay_ref[...]
    obs_weight = obs_weight_ref[...]
    rounded = state.astype(jnp.bfloat16)
    for step_index in range(STEPS):
        drift = (
            jnp.dot(rounded, transition_ref[...], preferred_element_type=jnp.float32)
            + current_ref[step_index] * drive
        )
        state = decay * state + jnp.tanh(drift)
        rounded = state.astype(jnp.bfloat16)
        predicted = jnp.dot(rounded, obs_matrix_ref[...], preferred_element_type=jnp.float32)
        misfit = predicted - observed_ref[step_index : step_index + 1, :]
        logw = logw - 0.5 * jnp.sum(obs_weight * misfit * misfit, axis=1, keepdims=True)
    state_out[...] = state
    rows_per_block = state.shape[0]
    full_state[pl.ds(pl.multiple_of(block * rows_per_block, rows_per_block), rows_per_block), :] = state

    @pl.when(block == 0)
    def _():
        peak_acc[...] = jnp.full(peak_acc.shape, -jnp.inf, jnp.float32)
        sum_acc[...] = jnp.zeros(sum_acc.shape, jnp.float32)
        weighted_acc[...] = jnp.zeros(weighted_acc.shape, jnp.float32)

    old_peak = peak_acc[...]
    new_peak = jnp.maximum(old_peak, jnp.max(logw, axis=0, keepdims=True))
    scale = jnp.exp(old_peak - new_peak)
    expw = jnp.exp(logw - new_peak[:, :1])
    sum_acc[...] = sum_acc[...] * scale + jnp.sum(expw, axis=0, keepdims=True)
    weighted_acc[...] = weighted_acc[...] * scale[:, :1] + jnp.sum(expw * state, axis=0, keepdims=True)
    peak_acc[...] = new_peak

    @pl.when(block == pl.num_programs(0) - 1)
    def _():
        lanes = peak_acc.shape[1]
        k = weighted_acc.shape[1] // lanes
        for row in range(k):
            message_out[row : row + 1, :] = weighted_acc[:, row * lanes : (row + 1) * lanes]
        message_out[k : k + 1, :] = sum_acc[...]
        message_out[k + 1 : k + 2, :] = peak_acc[...]
        rest = message_out.shape[0] - (k + 2)
        if rest:
            message_out[k + 2 :, :] = jnp.zeros((rest, lanes), jnp.float32)

        for pick_ref, rows_out in ((cycle_pick_ref, cycle_out), (pair_pick_ref, pair_out)):
            count = pick_ref.shape[0]

            def copy_row(j, carry, pick_ref=pick_ref, rows_out=rows_out):
                row = ancestors_ref[pick_ref[j]]
                rows_out[pl.ds(j, 1), :] = full_state[pl.ds(row, 1), :]
                return carry

            lax.fori_loop(0, count, copy_row, 0)
            rows_out[count : count + 1, 0:lanes] = sum_acc[...]
            rows_out[count : count + 1, lanes : 2 * lanes] = peak_acc[...]
            rows_out[count : count + 1, 2 * lanes :] = jnp.zeros((1, width_of(rows_out) - 2 * lanes), jnp.float32)


def width_of(ref):
    return ref.shape[1]


def run_steps(
    particles, log_prior, transition, drive_vector, current, decay_rate, obs_matrix, obs_weight, observed,
    ancestors, cycle_pick, pair_pick,
):
    rows, width = particles.shape
    n_obs = obs_matrix.shape[1]
    block = 256
    lanes = 128
    k = width // lanes
    message_rows = max(-(-(k + 2) // 8) * 8, 2 * k)
    n_cycle = cycle_pick.shape[0]
    n_pairs = pair_pick.shape[0]
    whole = lambda i: (0, 0)
    return pl.pallas_call(
        steps_kernel,
        grid=(rows // block,),
        in_specs=[
            pl.BlockSpec(memory_space=pltpu.SMEM),
            pl.BlockSpec(memory_space=pltpu.SMEM),
            pl.BlockSpec(memory_space=pltpu.SMEM),
            pl.BlockSpec(memory_space=pltpu.SMEM),
            pl.BlockSpec((block, width), lambda i: (i, 0)),
            pl.BlockSpec((block, 1), lambda i: (i, 0)),
            pl.BlockSpec((width, width), whole),
            pl.BlockSpec((1, width), whole),
            pl.BlockSpec((1, width), whole),
            pl.BlockSpec((width, n_obs), whole),
            pl.BlockSpec((1, n_obs), whole),
            pl.BlockSpec(observed.shape, whole),
        ],
        out_specs=[
            pl.BlockSpec((block, width), lambda i: (i, 0)),
            pl.BlockSpec((message_rows, lanes), whole),
            pl.BlockSpec((n_cycle + 1, width), whole),
            pl.BlockSpec((n_pairs + 1, width), whole),
        ],
        out_shape=[
            jax.ShapeDtypeStruct((rows, width), jnp.float32),
            jax.ShapeDtypeStruct((message_rows, lanes), jnp.float32),
            jax.ShapeDtypeStruct((n_cycle + 1, width), jnp.float32),
            jax.ShapeDtypeStruct((n_pairs + 1, width), jnp.float32),
        ],
        scratch_shapes=[
            pltpu.VMEM((1, lanes), jnp.float32),
            pltpu.VMEM((1, lanes), jnp.float32),
            pltpu.VMEM((1, width), jnp.float32),
            pltpu.VMEM((rows, width), jnp.float32),
        ],
        compiler_params=pltpu.CompilerParams(dimension_semantics=("arbitrary",)),
        cost_estimate=pl.CostEstimate(
            flops=2 * STEPS * rows * width * (width + n_obs),
            transcendentals=STEPS * rows * width,
            bytes_accessed=2 * rows * width * 4 + width * width * 2,
        ),
    )(
        current,
        ancestors,
        cycle_pick,
        pair_pick,
        particles,
        log_prior.reshape(rows, 1),
        transition,
        drive_vector.reshape(1, width),
        decay_rate.reshape(1, width),
        obs_matrix,
        obs_weight.reshape(1, n_obs),
        observed,
    )


def window(
    particles,
    log_prior,
    transition,
    drive_vector,
    current,
    decay_rate,
    obs_matrix,
    obs_weight,
    observed,
    ancestors,
    cycle_pick,
    pair_pick,
):
    state, message, cycle_out, pair_out = run_steps(
        particles, log_prior, transition, drive_vector, current, decay_rate, obs_matrix, obs_weight, observed,
        ancestors, cycle_pick, pair_pick,
    )
    n_blk = lax.axis_size(BLK)
    n_pair = lax.axis_size(PAIR)
    groups = n_blk * n_pair
    rows_here, width = state.shape
    n_cycle = cycle_pick.shape[0]
    n_pairs = pair_pick.shape[0]
    lanes = message.shape[1]
    k = width // lanes
    stamp = cycle_out[n_cycle : n_cycle + 1]

    cycle_in = shifted(cycle_out, BLK, 1)
    pair_in = shifted(pair_out, PAIR, n_pair // 2)

    pad = message.shape[0] - (k + 2)
    for axis, size in ((PAIR, n_pair), (BLK, n_blk)):
        bit = 1
        while bit < size:
            other = lax.ppermute(message, axis, [(i, i ^ bit) for i in range(size)])
            peak_row = jnp.maximum(message[k + 1], other[k + 1])
            mine_scale = jnp.exp(message[k + 1] - peak_row)
            other_scale = jnp.exp(other[k + 1] - peak_row)
            body = message[: k + 1] * mine_scale + other[: k + 1] * other_scale
            message = jnp.concatenate([body, peak_row[None], jnp.zeros((pad, lanes), jnp.float32)])
            bit *= 2
    total = message[k : k + 1]
    peak = message[k + 1 : k + 2]
    mean_state = (message[:k] / total).reshape(width)

    def group_weight(row):
        device_sum = row[:, :lanes]
        device_peak = row[:, lanes : 2 * lanes]
        return jnp.log(jnp.maximum(groups * (device_sum * jnp.exp(device_peak - peak)) / total, 0.1))

    own_w = group_weight(stamp)
    cycle_w = group_weight(cycle_in[n_cycle : n_cycle + 1])
    pair_w = group_weight(pair_in[n_pairs : n_pairs + 1])

    source = (
        ancestors.at[cycle_pick]
        .set(rows_here + jnp.arange(n_cycle, dtype=jnp.int32))
        .at[pair_pick]
        .set(rows_here + n_cycle + jnp.arange(n_pairs, dtype=jnp.int32))
    )
    table = jnp.concatenate([state, cycle_in[:n_cycle], pair_in[:n_pairs]], axis=0)
    migrated = table[source]
    tiles = source.reshape(rows_here // lanes, lanes)
    group_logw = jnp.where(
        tiles >= rows_here + n_cycle,
        pair_w,
        jnp.where(tiles >= rows_here, cycle_w, own_w),
    ).reshape(rows_here)
    return (migrated, group_logw, mean_state)


def solution(mesh):
    torus = Mesh(
        mesh.devices.reshape(2, 8, 2, 2, 4), ("blk_0", "blk_1", "blk_2", "pair_0", "pair_1")
    )
    in_specs = (
        P(BLK_PAIR, None),
        P(BLK_PAIR),
        P(),
        P(),
        P(),
        P(),
        P(),
        P(),
        P(),
        P(BLK_PAIR),
        P(BLK_PAIR),
        P(BLK_PAIR),
    )
    out_specs = (P(BLK_PAIR, None), P(BLK_PAIR), P())
    return jax.shard_map(window, mesh=torus, in_specs=in_specs, out_specs=out_specs, check_vma=False)
```

```python
import jax
import jax.numpy as jnp
from jax import lax
from jax.experimental import pallas as pl
from jax.experimental.pallas import tpu as pltpu
from jax.sharding import Mesh
from jax.sharding import PartitionSpec as P


STEPS = 4
BLK = ("blk_0", "blk_1", "blk_2")
PAIR = ("pair_0", "pair_1")
BLK_PAIR = ("blk_0", "blk_1", "blk_2", "pair_0", "pair_1")


def shifted(block, axis, distance):
    devices = range(lax.axis_size(axis))
    route = [((i - distance) % len(devices), i) for i in devices]
    return lax.ppermute(block, axis, route)


def steps_kernel(
    current_ref, state_ref, prior_ref, transition_ref, drive_ref, decay_ref,
    obs_matrix_ref, obs_weight_ref, observed_ref, state_out, message_out,
    peak_acc, sum_acc, weighted_acc,
):
    block = pl.program_id(0)
    state = state_ref[...]
    logw = prior_ref[...]
    drive = drive_ref[...]
    decay = decay_ref[...]
    obs_weight = obs_weight_ref[...]
    rounded = state.astype(jnp.bfloat16)
    for step_index in range(STEPS):
        drift = (
            jnp.dot(rounded, transition_ref[...], preferred_element_type=jnp.float32)
            + current_ref[step_index] * drive
        )
        state = decay * state + jnp.tanh(drift)
        rounded = state.astype(jnp.bfloat16)
        predicted = jnp.dot(rounded, obs_matrix_ref[...], preferred_element_type=jnp.float32)
        misfit = predicted - observed_ref[step_index : step_index + 1, :]
        logw = logw - 0.5 * jnp.sum(obs_weight * misfit * misfit, axis=1, keepdims=True)
    state_out[...] = state

    @pl.when(block == 0)
    def _():
        peak_acc[...] = jnp.full(peak_acc.shape, -jnp.inf, jnp.float32)
        sum_acc[...] = jnp.zeros(sum_acc.shape, jnp.float32)
        weighted_acc[...] = jnp.zeros(weighted_acc.shape, jnp.float32)

    old_peak = peak_acc[...]
    new_peak = jnp.maximum(old_peak, jnp.max(logw, axis=0, keepdims=True))
    scale = jnp.exp(old_peak - new_peak)
    expw = jnp.exp(logw - new_peak[:, :1])
    sum_acc[...] = sum_acc[...] * scale + jnp.sum(expw, axis=0, keepdims=True)
    weighted_acc[...] = weighted_acc[...] * scale[:, :1] + jnp.sum(expw * state, axis=0, keepdims=True)
    peak_acc[...] = new_peak

    @pl.when(block == pl.num_programs(0) - 1)
    def _():
        lanes = peak_acc.shape[1]
        k = weighted_acc.shape[1] // lanes
        for row in range(k):
            message_out[row : row + 1, :] = weighted_acc[:, row * lanes : (row + 1) * lanes]
        message_out[k : k + 1, :] = sum_acc[...]
        message_out[k + 1 : k + 2, :] = peak_acc[...]
        rest = message_out.shape[0] - (k + 2)
        if rest:
            message_out[k + 2 :, :] = jnp.zeros((rest, lanes), jnp.float32)


def run_steps(particles, log_prior, transition, drive_vector, current, decay_rate, obs_matrix, obs_weight, observed):
    rows, width = particles.shape
    n_obs = obs_matrix.shape[1]
    block = 256
    lanes = 128
    k = width // lanes
    message_rows = max(-(-(k + 2) // 8) * 8, 2 * k)
    whole = lambda i: (0, 0)
    return pl.pallas_call(
        steps_kernel,
        grid=(rows // block,),
        in_specs=[
            pl.BlockSpec(memory_space=pltpu.SMEM),
            pl.BlockSpec((block, width), lambda i: (i, 0)),
            pl.BlockSpec((block, 1), lambda i: (i, 0)),
            pl.BlockSpec((width, width), whole),
            pl.BlockSpec((1, width), whole),
            pl.BlockSpec((1, width), whole),
            pl.BlockSpec((width, n_obs), whole),
            pl.BlockSpec((1, n_obs), whole),
            pl.BlockSpec(observed.shape, whole),
        ],
        out_specs=[
            pl.BlockSpec((block, width), lambda i: (i, 0)),
            pl.BlockSpec((message_rows, lanes), whole),
        ],
        out_shape=[
            jax.ShapeDtypeStruct((rows, width), jnp.float32),
            jax.ShapeDtypeStruct((message_rows, lanes), jnp.float32),
        ],
        scratch_shapes=[
            pltpu.VMEM((1, lanes), jnp.float32),
            pltpu.VMEM((1, lanes), jnp.float32),
            pltpu.VMEM((1, width), jnp.float32),
        ],
        compiler_params=pltpu.CompilerParams(dimension_semantics=("arbitrary",)),
        cost_estimate=pl.CostEstimate(
            flops=2 * STEPS * rows * width * (width + n_obs),
            transcendentals=STEPS * rows * width,
            bytes_accessed=2 * rows * width * 4 + width * width * 2,
        ),
    )(
        current,
        particles,
        log_prior.reshape(rows, 1),
        transition,
        drive_vector.reshape(1, width),
        decay_rate.reshape(1, width),
        obs_matrix,
        obs_weight.reshape(1, n_obs),
        observed,
    )


def window(
    particles,
    log_prior,
    transition,
    drive_vector,
    current,
    decay_rate,
    obs_matrix,
    obs_weight,
    observed,
    ancestors,
    cycle_pick,
    pair_pick,
):
    state, message = run_steps(
        particles, log_prior, transition, drive_vector, current, decay_rate, obs_matrix, obs_weight, observed
    )
    n_blk = lax.axis_size(BLK)
    n_pair = lax.axis_size(PAIR)
    groups = n_blk * n_pair
    rows_here, width = state.shape
    n_cycle = cycle_pick.shape[0]
    n_pairs = pair_pick.shape[0]
    lanes = message.shape[1]
    k = width // lanes
    stamp = message[k : 2 * k].reshape(1, width)

    cycle_out = jnp.concatenate([state[ancestors[cycle_pick]], stamp])
    pair_out = jnp.concatenate([state[ancestors[pair_pick]], stamp])
    cycle_in = shifted(cycle_out, BLK, 1)
    pair_in = shifted(pair_out, PAIR, n_pair // 2)

    pad = message.shape[0] - (k + 2)

    def combine(mine, other):
        peak_row = jnp.maximum(mine[k + 1], other[k + 1])
        mine_scale = jnp.exp(mine[k + 1] - peak_row)
        other_scale = jnp.exp(other[k + 1] - peak_row)
        body = mine[: k + 1] * mine_scale + other[: k + 1] * other_scale
        return jnp.concatenate([body, peak_row[None], jnp.zeros((pad, lanes), jnp.float32)])

    def ring_of_four(message, axis):
        got = [lax.ppermute(message, axis, [(i, (i + s) % 4) for i in range(4)]) for s in (1, 2, 3)]
        even = lax.axis_index(axis) % 2 == 0
        own_pair = combine(message, jnp.where(even, got[2], got[0]))
        other_pair = combine(got[1], jnp.where(even, got[0], got[2]))
        return combine(own_pair, other_pair)

    def swap(message, axis, bit):
        size = lax.axis_size(axis)
        return combine(message, lax.ppermute(message, axis, [(i, i ^ bit) for i in range(size)]))

    stages = [
        lambda m: ring_of_four(m, "pair_1"),
        lambda m: ring_of_four(m, ("blk_0", "pair_0")),
        lambda m: swap(m, "blk_2", 1),
        lambda m: swap(m, "blk_1", 1),
        lambda m: swap(m, "blk_1", 2),
        lambda m: swap(m, "blk_1", 4),
    ]
    for stage in stages:
        message = stage(message)
    total = message[k : k + 1]
    peak = message[k + 1 : k + 2]
    mean_state = (message[:k] / total).reshape(width)

    def group_weight(row):
        device_sum = row[:, :lanes]
        device_peak = row[:, lanes : 2 * lanes]
        return jnp.log(jnp.maximum(groups * (device_sum * jnp.exp(device_peak - peak)) / total, 0.1))

    own_w = group_weight(stamp)
    cycle_w = group_weight(cycle_in[n_cycle : n_cycle + 1])
    pair_w = group_weight(pair_in[n_pairs : n_pairs + 1])

    source = (
        ancestors.at[cycle_pick]
        .set(rows_here + jnp.arange(n_cycle, dtype=jnp.int32))
        .at[pair_pick]
        .set(rows_here + n_cycle + jnp.arange(n_pairs, dtype=jnp.int32))
    )
    table = jnp.concatenate([state, cycle_in[:n_cycle], pair_in[:n_pairs]], axis=0)
    migrated = table[source]
    tiles = source.reshape(rows_here // lanes, lanes)
    group_logw = jnp.where(
        tiles >= rows_here + n_cycle,
        pair_w,
        jnp.where(tiles >= rows_here, cycle_w, own_w),
    ).reshape(rows_here)
    return (migrated, group_logw, mean_state)


def solution(mesh):
    torus = Mesh(
        mesh.devices.reshape(2, 8, 2, 2, 4), ("blk_0", "blk_1", "blk_2", "pair_0", "pair_1")
    )
    in_specs = (
        P(BLK_PAIR, None),
        P(BLK_PAIR),
        P(),
        P(),
        P(),
        P(),
        P(),
        P(),
        P(),
        P(BLK_PAIR),
        P(BLK_PAIR),
        P(BLK_PAIR),
    )
    out_specs = (P(BLK_PAIR, None), P(BLK_PAIR), P())
    return jax.shard_map(
        window, mesh=torus, in_specs=in_specs, out_specs=out_specs, check_vma=False
    )
```

```python
import jax
import jax.numpy as jnp
from jax import lax
from jax.experimental import pallas as pl
from jax.experimental.pallas import tpu as pltpu
from jax.sharding import Mesh
from jax.sharding import PartitionSpec as P


STEPS = 4
BLK = ("blk_0", "blk_1", "blk_2")
PAIR = ("pair_0", "pair_1")
BLK_PAIR = ("blk_0", "blk_1", "blk_2", "pair_0", "pair_1")


def shifted(block, axis, distance):
    devices = range(lax.axis_size(axis))
    route = [((i - distance) % len(devices), i) for i in devices]
    return lax.ppermute(block, axis, route)


def steps_kernel(
    current_ref, state_ref, prior_ref, transition_ref, drive_ref, decay_ref,
    obs_matrix_ref, obs_weight_ref, observed_ref, state_out, message_out,
    peak_acc, sum_acc, weighted_acc,
):
    block = pl.program_id(0)
    state = state_ref[...]
    logw = prior_ref[...]
    drive = drive_ref[...]
    decay = decay_ref[...]
    obs_weight = obs_weight_ref[...]
    rounded = state.astype(jnp.bfloat16)
    for step_index in range(STEPS):
        drift = (
            jnp.dot(rounded, transition_ref[...], preferred_element_type=jnp.float32)
            + current_ref[step_index] * drive
        )
        state = decay * state + jnp.tanh(drift)
        rounded = state.astype(jnp.bfloat16)
        predicted = jnp.dot(rounded, obs_matrix_ref[...], preferred_element_type=jnp.float32)
        misfit = predicted - observed_ref[step_index : step_index + 1, :]
        logw = logw - 0.5 * jnp.sum(obs_weight * misfit * misfit, axis=1, keepdims=True)
    state_out[...] = state

    @pl.when(block == 0)
    def _():
        peak_acc[...] = jnp.full(peak_acc.shape, -jnp.inf, jnp.float32)
        sum_acc[...] = jnp.zeros(sum_acc.shape, jnp.float32)
        weighted_acc[...] = jnp.zeros(weighted_acc.shape, jnp.float32)

    old_peak = peak_acc[...]
    new_peak = jnp.maximum(old_peak, jnp.max(logw, axis=0, keepdims=True))
    scale = jnp.exp(old_peak - new_peak)
    expw = jnp.exp(logw - new_peak[:, :1])
    sum_acc[...] = sum_acc[...] * scale + jnp.sum(expw, axis=0, keepdims=True)
    weighted_acc[...] = weighted_acc[...] * scale[:, :1] + jnp.sum(expw * state, axis=0, keepdims=True)
    peak_acc[...] = new_peak

    @pl.when(block == pl.num_programs(0) - 1)
    def _():
        lanes = peak_acc.shape[1]
        k = weighted_acc.shape[1] // lanes
        for row in range(k):
            message_out[row : row + 1, :] = weighted_acc[:, row * lanes : (row + 1) * lanes]
        message_out[k : k + 1, :] = sum_acc[...]
        message_out[k + 1 : k + 2, :] = peak_acc[...]
        rest = message_out.shape[0] - (k + 2)
        if rest:
            message_out[k + 2 :, :] = jnp.zeros((rest, lanes), jnp.float32)


def run_steps(particles, log_prior, transition, drive_vector, current, decay_rate, obs_matrix, obs_weight, observed):
    rows, width = particles.shape
    n_obs = obs_matrix.shape[1]
    block = 1024
    lanes = 128
    k = width // lanes
    message_rows = max(-(-(k + 2) // 8) * 8, 2 * k)
    whole = lambda i: (0, 0)
    return pl.pallas_call(
        steps_kernel,
        grid=(rows // block,),
        in_specs=[
            pl.BlockSpec(memory_space=pltpu.SMEM),
            pl.BlockSpec((block, width), lambda i: (i, 0)),
            pl.BlockSpec((block, 1), lambda i: (i, 0)),
            pl.BlockSpec((width, width), whole),
            pl.BlockSpec((1, width), whole),
            pl.BlockSpec((1, width), whole),
            pl.BlockSpec((width, n_obs), whole),
            pl.BlockSpec((1, n_obs), whole),
            pl.BlockSpec(observed.shape, whole),
        ],
        out_specs=[
            pl.BlockSpec((block, width), lambda i: (i, 0)),
            pl.BlockSpec((message_rows, lanes), whole),
        ],
        out_shape=[
            jax.ShapeDtypeStruct((rows, width), jnp.float32),
            jax.ShapeDtypeStruct((message_rows, lanes), jnp.float32),
        ],
        scratch_shapes=[
            pltpu.VMEM((1, lanes), jnp.float32),
            pltpu.VMEM((1, lanes), jnp.float32),
            pltpu.VMEM((1, width), jnp.float32),
        ],
        compiler_params=pltpu.CompilerParams(dimension_semantics=("arbitrary",)),
        cost_estimate=pl.CostEstimate(
            flops=2 * STEPS * rows * width * (width + n_obs),
            transcendentals=STEPS * rows * width,
            bytes_accessed=2 * rows * width * 4 + width * width * 2,
        ),
    )(
        current,
        particles,
        log_prior.reshape(rows, 1),
        transition,
        drive_vector.reshape(1, width),
        decay_rate.reshape(1, width),
        obs_matrix,
        obs_weight.reshape(1, n_obs),
        observed,
    )


def window(
    particles,
    log_prior,
    transition,
    drive_vector,
    current,
    decay_rate,
    obs_matrix,
    obs_weight,
    observed,
    ancestors,
    cycle_pick,
    pair_pick,
):
    state, message = run_steps(
        particles, log_prior, transition, drive_vector, current, decay_rate, obs_matrix, obs_weight, observed
    )
    n_blk = lax.axis_size(BLK)
    n_pair = lax.axis_size(PAIR)
    groups = n_blk * n_pair
    rows_here, width = state.shape
    n_cycle = cycle_pick.shape[0]
    n_pairs = pair_pick.shape[0]
    lanes = message.shape[1]
    k = width // lanes
    stamp = message[k : 2 * k].reshape(1, width)

    cycle_out = jnp.concatenate([state[ancestors[cycle_pick]], stamp])
    pair_out = jnp.concatenate([state[ancestors[pair_pick]], stamp])
    cycle_in = shifted(cycle_out, BLK, 1)
    pair_in = shifted(pair_out, PAIR, n_pair // 2)

    pad = message.shape[0] - (k + 2)
    for axis, size in ((PAIR, n_pair), (BLK, n_blk)):
        bit = 1
        while bit < size:
            other = lax.ppermute(message, axis, [(i, i ^ bit) for i in range(size)])
            peak_row = jnp.maximum(message[k + 1], other[k + 1])
            mine_scale = jnp.exp(message[k + 1] - peak_row)
            other_scale = jnp.exp(other[k + 1] - peak_row)
            body = message[: k + 1] * mine_scale + other[: k + 1] * other_scale
            message = jnp.concatenate([body, peak_row[None], jnp.zeros((pad, lanes), jnp.float32)])
            bit *= 2
    total = message[k : k + 1]
    peak = message[k + 1 : k + 2]
    mean_state = (message[:k] / total).reshape(width)

    def group_weight(row):
        device_sum = row[:, :lanes]
        device_peak = row[:, lanes : 2 * lanes]
        return jnp.log(jnp.maximum(groups * (device_sum * jnp.exp(device_peak - peak)) / total, 0.1))

    own_w = group_weight(stamp)
    cycle_w = group_weight(cycle_in[n_cycle : n_cycle + 1])
    pair_w = group_weight(pair_in[n_pairs : n_pairs + 1])

    source = (
        ancestors.at[cycle_pick]
        .set(rows_here + jnp.arange(n_cycle, dtype=jnp.int32))
        .at[pair_pick]
        .set(rows_here + n_cycle + jnp.arange(n_pairs, dtype=jnp.int32))
    )
    table = jnp.concatenate([state, cycle_in[:n_cycle], pair_in[:n_pairs]], axis=0)
    migrated = table[source]
    tiles = source.reshape(rows_here // lanes, lanes)
    group_logw = jnp.where(
        tiles >= rows_here + n_cycle,
        pair_w,
        jnp.where(tiles >= rows_here, cycle_w, own_w),
    ).reshape(rows_here)
    return (migrated, group_logw, mean_state)


def solution(mesh):
    torus = Mesh(
        mesh.devices.reshape(2, 8, 2, 2, 4), ("blk_0", "blk_1", "blk_2", "pair_0", "pair_1")
    )
    in_specs = (
        P(BLK_PAIR, None),
        P(BLK_PAIR),
        P(),
        P(),
        P(),
        P(),
        P(),
        P(),
        P(),
        P(BLK_PAIR),
        P(BLK_PAIR),
        P(BLK_PAIR),
    )
    out_specs = (P(BLK_PAIR, None), P(BLK_PAIR), P())
    return jax.shard_map(
        window, mesh=torus, in_specs=in_specs, out_specs=out_specs, check_vma=False
    )
```
